128 devices in a mesh: shot: 4 (over z_hi, core), rcv: 32 (over x, y, z_lo).
Axes of the slice: x: 4, y: 4, z: 4 (z_hi: 2, z_lo: 2; z = z_hi * 2 + z_lo), core: 2. Of those that a mesh axis runs over, the one named last changes fastest.
Arguments:
- data: float32 [1, 2, 8192, 1024], P(None, None, 'rcv', 'shot'), may hold values from -6 to 6
- impulse: float32 [1, 2, 8192, 8192], P(None, None, 'rcv'), may hold values from -0.0625 to 0.0625
- wavelet: float32 [1, 2], replicated, may hold values from -96 to 96
- live: int32 [8192, 1024], P('rcv', 'shot'), may hold values from 0 to 1, as said below
Outputs:
- residual: float32 [1, 2, 8192, 1024], P(None, None, 'rcv', 'shot')
- gradient: float32 [1, 2, 8192, 8192], P(None, None, 'rcv', 'shot')
The draws below stay inside these ranges and needn't reach their ends.
Inputs may be any that keep to these rules, and one draw needn't show every extreme that they name: live[r, s] is 0 where |r - s * 8| is at most a per-shot half gap of 1 to 4 positions, and at scattered dead traces; 1 elsewhere.
All inputs are finite; a program needn't handle non-finite values.
Results may differ from the reference program's by a relative error of at most 0.000084.
Values sent between devices are 32-bit elements; how exact they have to be, the bound alone decides.
No kernel may reach another device: no remote copies, remote signals or barrier semaphores. Data moves between devices by JAX's collectives and lax.ppermute only.
A program may use at most 192 MiB of HBM per device.

```python
import jax
import jax.numpy as jnp
from jax import lax

NR = 8192
FREQS = 1
NS = 1024


def draw_live(key, part):
    key_gap, key_dead = jax.random.split(jax.random.fold_in(key, 7))
    rows = lax.broadcasted_iota(jnp.int32, (NR, NS), 0)
    cols = lax.broadcasted_iota(jnp.int32, (NR, NS), 1)
    centre = cols * (NR // NS)
    gaps = jax.random.randint(key_gap, (1, NS), 1, 5)
    near = jnp.abs(rows - centre) <= gaps
    dead = jax.random.randint(key_dead, (NR, NS), 0, 25) == 0
    return jnp.where(near | dead, 0, 1).astype(jnp.int32)


def steps_of(key, dims, cuts, least, largest):
    loudness, own = 1.0, jax.random.fold_in(key, 6)
    for axis_at, blocks in cuts:
        draws = jnp.exp(jax.random.uniform(jax.random.fold_in(own, axis_at), (blocks,), jnp.float32, least / len(cuts), largest / len(cuts)))
        loudness = loudness * jnp.repeat(draws, dims[axis_at] // blocks).reshape([-1 if axis == axis_at else 1 for axis in range(len(dims))])
    return loudness


def normal_values(rng, dims, deviation, reach, pieces=(), dtype=jnp.bfloat16):
    loudness = steps_of(rng, dims, pieces, -0.22, 0.18) if pieces else 1.0
    result = jax.random.normal(rng, dims, jnp.float32) * deviation * loudness
    return jnp.minimum(jnp.maximum(result, -reach), reach).astype(dtype)


def setup_inputs(seed: int = 0) -> dict:
    key_list = jax.random.split(jax.random.key(seed), 5)
    data = normal_values(key_list[0], (FREQS, 2, NR, NS), 1.0, 6.0, ((2, 32), (3, 4)), jnp.float32)
    impulse = normal_values(key_list[1], (FREQS, 2, NR, NR), NR ** -0.5, 0.0625, ((2, 32),), jnp.float32)
    wavelet = normal_values(key_list[2], (FREQS, 2), 16.0, 96.0, (), jnp.float32)
    live = draw_live(jax.random.fold_in(key_list[4], 71), 0)
    return dict(data=data, impulse=impulse, wavelet=wavelet, live=live)


def product(left, right, form):
    return jnp.einsum(form, left, right, precision=lax.Precision.HIGHEST, preferred_element_type=jnp.float32)


def reference(data, impulse, wavelet, live):
    mask = live.astype(jnp.float32)
    observed = data * mask[None, None]
    rows = lax.broadcasted_iota(jnp.int32, (NR, NS), 0)
    cols = lax.broadcasted_iota(jnp.int32, (NR, NS), 1)
    source = (rows == cols * (NR // NS)).astype(jnp.float32)
    panel_re = wavelet[:, 0][:, None, None] * source[None] - observed[:, 0]
    panel_im = wavelet[:, 1][:, None, None] * source[None] - observed[:, 1]
    imp_re = impulse[:, 0]
    imp_im = impulse[:, 1]
    pred_re = product(imp_re, panel_re, "frk,fks->frs") - product(imp_im, panel_im, "frk,fks->frs")
    pred_im = product(imp_re, panel_im, "frk,fks->frs") + product(imp_im, panel_re, "frk,fks->frs")
    res_re = mask[None] * (observed[:, 0] - pred_re)
    res_im = mask[None] * (observed[:, 1] - pred_im)
    residual = jnp.stack([res_re, res_im], axis=1)
    scale = -(NS ** -0.5)
    grad_re = product(res_re, panel_re, "frs,fks->frk") + product(res_im, panel_im, "frs,fks->frk")
    grad_im = product(res_im, panel_re, "frs,fks->frk") - product(res_re, panel_im, "frs,fks->frk")
    gradient = jnp.stack([grad_re, grad_im], axis=1) * scale
    return (residual, gradient)
```

```python
import jax
import jax.numpy as jnp
from jax import lax
from jax.sharding import Mesh, PartitionSpec as P

RCV = ("x", "y", "zl")
SHOT = ("zh", "c")


def product(left, right, form):
    return jnp.einsum(form, left, right, precision=lax.Precision.HIGH, preferred_element_type=jnp.float32)


def convolve(impulse_cols, panel):
    left_re = impulse_cols[:, 0]
    left_im = impulse_cols[:, 1]
    right_re = panel[:, 0]
    right_im = panel[:, 1]
    out_re = product(left_re, right_re, "frk,fks->frs") - product(left_im, right_im, "frk,fks->frs")
    out_im = product(left_re, right_im, "frk,fks->frs") + product(left_im, right_re, "frk,fks->frs")
    return jnp.stack([out_re, out_im], axis=1)


def correlate(residual, panel, scale):
    res_re = residual[:, 0]
    res_im = residual[:, 1]
    pan_re = panel[:, 0]
    pan_im = panel[:, 1]
    out_re = product(res_re, pan_re, "frs,fks->frk") + product(res_im, pan_im, "frs,fks->frk")
    out_im = product(res_im, pan_re, "frs,fks->frk") - product(res_re, pan_im, "frs,fks->frk")
    return jnp.stack([out_re, out_im], axis=1) * scale


def make_panel(data, wavelet, live, total_shots, positions):
    rows_dev = data.shape[2]
    shots_dev = data.shape[3]
    spacing = positions // total_shots
    mask = live.astype(jnp.float32)
    observed = data * mask[None, None]
    rcv_idx = (lax.axis_index("x") * lax.axis_size("y") + lax.axis_index("y")) * lax.axis_size("zl") + lax.axis_index("zl")
    shot_idx = lax.axis_index("zh") * lax.axis_size("c") + lax.axis_index("c")
    row_ids = rcv_idx * rows_dev + lax.broadcasted_iota(jnp.int32, (rows_dev, shots_dev), 0)
    col_ids = shot_idx * shots_dev + lax.broadcasted_iota(jnp.int32, (rows_dev, shots_dev), 1)
    source = (row_ids == col_ids * spacing).astype(jnp.float32)
    panel = wavelet[:, :, None, None] * source[None, None] - observed
    return mask, observed, panel


def fine_mesh(mesh):
    n_rcv = mesh.shape["rcv"]
    n_shot = mesh.shape["shot"]
    devs = mesh.devices.reshape(2, n_shot // 2, 4, 4, n_rcv // 16)
    return Mesh(devs, ("zh", "c", "x", "y", "zl"))


def local(data, impulse, wavelet, live):
    positions = impulse.shape[3]
    total_shots = data.shape[3] * lax.axis_size(SHOT)
    scale = -(total_shots ** (-0.5))
    mask, observed, panel = make_panel(data, wavelet, live, total_shots, positions)
    g = lax.all_gather(panel, "zl", axis=2, tiled=True)
    g = lax.all_gather(g, "y", axis=2, tiled=True)
    g = lax.all_gather(g, "x", axis=2, tiled=True)
    predicted = convolve(impulse, g)
    residual = mask[None, None] * (observed - predicted)
    terms = correlate(residual, g, scale)
    gradient = lax.psum_scatter(terms, SHOT, scatter_dimension=3, tiled=True)
    return (residual, gradient)


def solution(mesh):
    m = fine_mesh(mesh)
    placed = (P(None, None, RCV, SHOT), P(None, None, RCV, None), P(), P(RCV, SHOT))
    return jax.shard_map(local, mesh=m, in_specs=placed,
                         out_specs=(P(None, None, RCV, SHOT), P(None, None, RCV, SHOT)), check_vma=False)
```

```python
import jax
import jax.numpy as jnp
from jax import lax
from jax.sharding import Mesh, PartitionSpec as P

RCV = ("x", "y", "zl")
SHOT = ("zh", "c")


def product(left, right, form):
    return jnp.einsum(form, left, right, precision=lax.Precision.HIGH, preferred_element_type=jnp.float32)


def convolve(impulse_cols, panel):
    left_re = impulse_cols[:, 0]
    left_im = impulse_cols[:, 1]
    right_re = panel[:, 0]
    right_im = panel[:, 1]
    out_re = product(left_re, right_re, "frk,fks->frs") - product(left_im, right_im, "frk,fks->frs")
    out_im = product(left_re, right_im, "frk,fks->frs") + product(left_im, right_re, "frk,fks->frs")
    return jnp.stack([out_re, out_im], axis=1)


def correlate(residual, panel, scale):
    res_re = residual[:, 0]
    res_im = residual[:, 1]
    pan_re = panel[:, 0]
    pan_im = panel[:, 1]
    out_re = product(res_re, pan_re, "frs,fks->frk") + product(res_im, pan_im, "frs,fks->frk")
    out_im = product(res_im, pan_re, "frs,fks->frk") - product(res_re, pan_im, "frs,fks->frk")
    return jnp.stack([out_re, out_im], axis=1) * scale


def make_panel(data, wavelet, live, total_shots, positions):
    rows_dev = data.shape[2]
    shots_dev = data.shape[3]
    spacing = positions // total_shots
    mask = live.astype(jnp.float32)
    observed = data * mask[None, None]
    rcv_idx = (lax.axis_index("x") * lax.axis_size("y") + lax.axis_index("y")) * lax.axis_size("zl") + lax.axis_index("zl")
    shot_idx = lax.axis_index("zh") * lax.axis_size("c") + lax.axis_index("c")
    row_ids = rcv_idx * rows_dev + lax.broadcasted_iota(jnp.int32, (rows_dev, shots_dev), 0)
    col_ids = shot_idx * shots_dev + lax.broadcasted_iota(jnp.int32, (rows_dev, shots_dev), 1)
    source = (row_ids == col_ids * spacing).astype(jnp.float32)
    panel = wavelet[:, :, None, None] * source[None, None] - observed
    return mask, observed, panel


def fine_mesh(mesh):
    n_rcv = mesh.shape["rcv"]
    n_shot = mesh.shape["shot"]
    devs = mesh.devices.reshape(2, n_shot // 2, 4, 4, n_rcv // 16)
    return Mesh(devs, ("zh", "c", "x", "y", "zl"))


def ring_gather(block, axis_name, split_axis):
    n = lax.axis_size(axis_name)
    i = lax.axis_index(axis_name)
    fwd = [(s, (s + 1) % n) for s in range(n)]
    bwd = [(s, (s - 1) % n) for s in range(n)]
    left = lax.ppermute(block, axis_name, fwd)
    right = lax.ppermute(block, axis_name, bwd)
    h = block.shape[split_axis] // 2
    far_a = lax.ppermute(lax.slice_in_dim(right, 0, h, axis=split_axis), axis_name, bwd)
    far_b = lax.ppermute(lax.slice_in_dim(left, h, 2 * h, axis=split_axis), axis_name, fwd)
    far = jnp.concatenate([far_a, far_b], axis=split_axis)
    by_offset = jnp.stack([block, right, far, left])
    idx = (jnp.arange(n, dtype=jnp.int32) - i) % n
    return jnp.take(by_offset, idx, axis=0)


def local(data, impulse, wavelet, live):
    positions = impulse.shape[3]
    total_shots = data.shape[3] * lax.axis_size(SHOT)
    scale = -(total_shots ** (-0.5))
    mask, observed, panel = make_panel(data, wavelet, live, total_shots, positions)
    g = lax.all_gather(panel, "zl", axis=2, tiled=True)
    g_re = lax.all_gather(g[:, 0], "y", axis=1, tiled=True)
    g_re = lax.all_gather(g_re, "x", axis=1, tiled=True)
    f, rows2, cols = g[:, 1].shape
    gx = ring_gather(g[:, 1], "x", 1)
    gy = ring_gather(gx, "y", 0)
    g_im = gy.transpose(2, 1, 0, 3, 4).reshape(f, 16 * rows2, cols)
    g = jnp.stack([g_re, g_im], axis=1)
    predicted = convolve(impulse, g)
    residual = mask[None, None] * (observed - predicted)
    terms = correlate(residual, g, scale)
    gradient = lax.psum_scatter(terms, SHOT, scatter_dimension=3, tiled=True)
    return (residual, gradient)


def solution(mesh):
    m = fine_mesh(mesh)
    placed = (P(None, None, RCV, SHOT), P(None, None, RCV, None), P(), P(RCV, SHOT))
    return jax.shard_map(local, mesh=m, in_specs=placed,
                         out_specs=(P(None, None, RCV, SHOT), P(None, None, RCV, SHOT)), check_vma=False)
```

```python
import jax
import jax.numpy as jnp
from jax import lax
from jax.sharding import Mesh, PartitionSpec as P

RCV = ("x", "y", "zl")
SHOT = ("zh", "c")


def product(left, right, form):
    return jnp.einsum(form, left, right, precision=lax.Precision.HIGH, preferred_element_type=jnp.float32)


def convolve(impulse_cols, panel):
    left_re = impulse_cols[:, 0]
    left_im = impulse_cols[:, 1]
    right_re = panel[:, 0]
    right_im = panel[:, 1]
    out_re = product(left_re, right_re, "frk,fks->frs") - product(left_im, right_im, "frk,fks->frs")
    out_im = product(left_re, right_im, "frk,fks->frs") + product(left_im, right_re, "frk,fks->frs")
    return jnp.stack([out_re, out_im], axis=1)


def correlate(residual, panel, scale):
    res_re = residual[:, 0]
    res_im = residual[:, 1]
    pan_re = panel[:, 0]
    pan_im = panel[:, 1]
    out_re = product(res_re, pan_re, "frs,fks->frk") + product(res_im, pan_im, "frs,fks->frk")
    out_im = product(res_im, pan_re, "frs,fks->frk") - product(res_re, pan_im, "frs,fks->frk")
    return jnp.stack([out_re, out_im], axis=1) * scale


def make_panel(data, wavelet, live, total_shots, positions):
    rows_dev = data.shape[2]
    shots_dev = data.shape[3]
    spacing = positions // total_shots
    mask = live.astype(jnp.float32)
    observed = data * mask[None, None]
    rcv_idx = (lax.axis_index("x") * lax.axis_size("y") + lax.axis_index("y")) * lax.axis_size("zl") + lax.axis_index("zl")
    shot_idx = lax.axis_index("zh") * lax.axis_size("c") + lax.axis_index("c")
    row_ids = rcv_idx * rows_dev + lax.broadcasted_iota(jnp.int32, (rows_dev, shots_dev), 0)
    col_ids = shot_idx * shots_dev + lax.broadcasted_iota(jnp.int32, (rows_dev, shots_dev), 1)
    source = (row_ids == col_ids * spacing).astype(jnp.float32)
    panel = wavelet[:, :, None, None] * source[None, None] - observed
    return mask, observed, panel


def fine_mesh(mesh):
    n_rcv = mesh.shape["rcv"]
    n_shot = mesh.shape["shot"]
    devs = mesh.devices.reshape(2, n_shot // 2, 4, 4, n_rcv // 16)
    return Mesh(devs, ("zh", "c", "x", "y", "zl"))


def ring_gather(block, axis_name, axis, split_axis):
    n = lax.axis_size(axis_name)
    i = lax.axis_index(axis_name)
    fwd = [(s, (s + 1) % n) for s in range(n)]
    bwd = [(s, (s - 1) % n) for s in range(n)]
    left = lax.ppermute(block, axis_name, fwd)
    right = lax.ppermute(block, axis_name, bwd)
    h = block.shape[split_axis] // 2
    far_a = lax.ppermute(lax.slice_in_dim(right, 0, h, axis=split_axis), axis_name, bwd)
    far_b = lax.ppermute(lax.slice_in_dim(left, h, 2 * h, axis=split_axis), axis_name, fwd)
    shape = list(block.shape)
    shape[axis] = n
    buf = jnp.zeros(shape, block.dtype)

    def at(part, slot, offset):
        starts = [0] * len(shape)
        starts[axis] = slot
        starts[split_axis] = offset
        return lax.dynamic_update_slice(buf_ref[0], part, starts)

    buf_ref = [buf]
    for part, slot, offset in ((block, i, 0), (right, (i + 1) % n, 0), (left, (i + n - 1) % n, 0),
                               (far_a, (i + 2) % n, 0), (far_b, (i + 2) % n, h)):
        buf_ref[0] = at(part, slot, offset)
    return buf_ref[0]


def local(data, impulse, wavelet, live):
    positions = impulse.shape[3]
    total_shots = data.shape[3] * lax.axis_size(SHOT)
    scale = -(total_shots ** (-0.5))
    mask, observed, panel = make_panel(data, wavelet, live, total_shots, positions)
    g = lax.all_gather(panel, "zl", axis=2, tiled=True)
    g_re = lax.all_gather(g[:, 0], "y", axis=1, tiled=True)
    g_re = lax.all_gather(g_re, "x", axis=1, tiled=True)
    f, rows2, cols = g[:, 1].shape
    gx = ring_gather(g[:, 1].reshape(f, 1, 1, rows2, cols), "x", 1, 3)
    gy = ring_gather(gx, "y", 2, 1)
    g_im = gy.reshape(f, 16 * rows2, cols)
    g = jnp.stack([g_re, g_im], axis=1)
    predicted = convolve(impulse, g)
    residual = mask[None, None] * (observed - predicted)
    lhs_re = jnp.concatenate([residual[:, 0], residual[:, 1]], axis=1) * scale
    lhs_im = jnp.concatenate([residual[:, 1], -residual[:, 0]], axis=1) * scale
    terms = product(lhs_re, g[:, 0], "frs,fks->frk") + product(lhs_im, g[:, 1], "frs,fks->frk")
    terms = terms.reshape(terms.shape[0], 2, terms.shape[1] // 2, terms.shape[2])
    gradient = lax.psum_scatter(terms, SHOT, scatter_dimension=3, tiled=True)
    return (residual, gradient)


def solution(mesh):
    m = fine_mesh(mesh)
    placed = (P(None, None, RCV, SHOT), P(None, None, RCV, None), P(), P(RCV, SHOT))
    return jax.shard_map(local, mesh=m, in_specs=placed,
                         out_specs=(P(None, None, RCV, SHOT), P(None, None, RCV, SHOT)), check_vma=False)
```

```python
import jax
import jax.numpy as jnp
from jax import lax
from jax.sharding import Mesh, PartitionSpec as P

RCV = ("x", "y", "zl")
SHOT = ("zh", "c")


def product(left, right, form):
    return jnp.einsum(form, left, right, precision=lax.Precision.HIGH, preferred_element_type=jnp.float32)


def convolve(impulse_cols, panel):
    left_re = impulse_cols[:, 0]
    left_im = impulse_cols[:, 1]
    right_re = panel[:, 0]
    right_im = panel[:, 1]
    out_re = product(left_re, right_re, "frk,fks->frs") - product(left_im, right_im, "frk,fks->frs")
    out_im = product(left_re, right_im, "frk,fks->frs") + product(left_im, right_re, "frk,fks->frs")
    return jnp.stack([out_re, out_im], axis=1)


def correlate(residual, panel, scale):
    res_re = residual[:, 0]
    res_im = residual[:, 1]
    pan_re = panel[:, 0]
    pan_im = panel[:, 1]
    out_re = product(res_re, pan_re, "frs,fks->frk") + product(res_im, pan_im, "frs,fks->frk")
    out_im = product(res_im, pan_re, "frs,fks->frk") - product(res_re, pan_im, "frs,fks->frk")
    return jnp.stack([out_re, out_im], axis=1) * scale


def make_panel(data, wavelet, live, total_shots, positions):
    rows_dev = data.shape[2]
    shots_dev = data.shape[3]
    spacing = positions // total_shots
    mask = live.astype(jnp.float32)
    observed = data * mask[None, None]
    rcv_idx = (lax.axis_index("x") * lax.axis_size("y") + lax.axis_index("y")) * lax.axis_size("zl") + lax.axis_index("zl")
    shot_idx = lax.axis_index("zh") * lax.axis_size("c") + lax.axis_index("c")
    row_ids = rcv_idx * rows_dev + lax.broadcasted_iota(jnp.int32, (rows_dev, shots_dev), 0)
    col_ids = shot_idx * shots_dev + lax.broadcasted_iota(jnp.int32, (rows_dev, shots_dev), 1)
    source = (row_ids == col_ids * spacing).astype(jnp.float32)
    panel = wavelet[:, :, None, None] * source[None, None] - observed
    return mask, observed, panel


def fine_mesh(mesh):
    n_rcv = mesh.shape["rcv"]
    n_shot = mesh.shape["shot"]
    devs = mesh.devices.reshape(2, n_shot // 2, 4, 4, n_rcv // 16)
    return Mesh(devs, ("zh", "c", "x", "y", "zl"))


def ring_gather(block, axis_name, axis, split_axis):
    n = lax.axis_size(axis_name)
    i = lax.axis_index(axis_name)
    fwd = [(s, (s + 1) % n) for s in range(n)]
    bwd = [(s, (s - 1) % n) for s in range(n)]
    left = lax.ppermute(block, axis_name, fwd)
    right = lax.ppermute(block, axis_name, bwd)
    h = block.shape[split_axis] // 2
    far_a = lax.ppermute(lax.slice_in_dim(right, 0, h, axis=split_axis), axis_name, bwd)
    far_b = lax.ppermute(lax.slice_in_dim(left, h, 2 * h, axis=split_axis), axis_name, fwd)
    shape = list(block.shape)
    shape[axis] = n
    buf = jnp.zeros(shape, block.dtype)

    def at(part, slot, offset):
        starts = [0] * len(shape)
        starts[axis] = slot
        starts[split_axis] = offset
        return lax.dynamic_update_slice(buf_ref[0], part, starts)

    buf_ref = [buf]
    for part, slot, offset in ((block, i, 0), (right, (i + 1) % n, 0), (left, (i + n - 1) % n, 0),
                               (far_a, (i + 2) % n, 0), (far_b, (i + 2) % n, h)):
        buf_ref[0] = at(part, slot, offset)
    return buf_ref[0]


def pair_gather(block, axis_name, axis):
    i = lax.axis_index(axis_name)
    other = lax.ppermute(block, axis_name, [(0, 1), (1, 0)])
    shape = list(block.shape)
    blk = shape[axis]
    shape[axis] = 2 * blk
    starts = [0] * len(shape)
    buf = jnp.zeros(shape, block.dtype)
    starts[axis] = i * blk
    buf = lax.dynamic_update_slice(buf, block, starts)
    starts[axis] = (1 - i) * blk
    return lax.dynamic_update_slice(buf, other, starts)


def local(data, impulse, wavelet, live):
    positions = impulse.shape[3]
    total_shots = data.shape[3] * lax.axis_size(SHOT)
    scale = -(total_shots ** (-0.5))
    mask, observed, panel = make_panel(data, wavelet, live, total_shots, positions)
    g = pair_gather(panel, "zl", 2)
    g_re = lax.all_gather(g[:, 0], "y", axis=1, tiled=True)
    g_re = lax.all_gather(g_re, "x", axis=1, tiled=True)
    f, rows2, cols = g[:, 1].shape
    gx = ring_gather(g[:, 1].reshape(f, 1, 1, rows2, cols), "x", 1, 3)
    gy = ring_gather(gx, "y", 2, 1)
    g_im = gy.reshape(f, 16 * rows2, cols)
    g = jnp.stack([g_re, g_im], axis=1)
    predicted = convolve(impulse, g)
    residual = mask[None, None] * (observed - predicted)
    lhs_re = jnp.concatenate([residual[:, 0], residual[:, 1]], axis=1) * scale
    lhs_im = jnp.concatenate([residual[:, 1], -residual[:, 0]], axis=1) * scale
    terms = product(lhs_re, g[:, 0], "frs,fks->frk") + product(lhs_im, g[:, 1], "frs,fks->frk")
    terms = terms.reshape(terms.shape[0], 2, terms.shape[1] // 2, terms.shape[2])
    gradient = lax.psum_scatter(terms, SHOT, scatter_dimension=3, tiled=True)
    return (residual, gradient)


def solution(mesh):
    m = fine_mesh(mesh)
    placed = (P(None, None, RCV, SHOT), P(None, None, RCV, None), P(), P(RCV, SHOT))
    return jax.shard_map(local, mesh=m, in_specs=placed,
                         out_specs=(P(None, None, RCV, SHOT), P(None, None, RCV, SHOT)), check_vma=False)
```

```python
import jax
import jax.numpy as jnp
from jax import lax
from jax.sharding import Mesh, PartitionSpec as P

RCV = ("x", "y", "zl")
SHOT = ("zh", "c")


def product(left, right, form):
    return jnp.einsum(form, left, right, precision=lax.Precision.HIGH, preferred_element_type=jnp.float32)


def convolve(impulse_cols, panel):
    left_re = impulse_cols[:, 0]
    left_im = impulse_cols[:, 1]
    right_re = panel[:, 0]
    right_im = panel[:, 1]
    out_re = product(left_re, right_re, "frk,fks->frs") - product(left_im, right_im, "frk,fks->frs")
    out_im = product(left_re, right_im, "frk,fks->frs") + product(left_im, right_re, "frk,fks->frs")
    return jnp.stack([out_re, out_im], axis=1)


def correlate(residual, panel, scale):
    res_re = residual[:, 0]
    res_im = residual[:, 1]
    pan_re = panel[:, 0]
    pan_im = panel[:, 1]
    out_re = product(res_re, pan_re, "frs,fks->frk") + product(res_im, pan_im, "frs,fks->frk")
    out_im = product(res_im, pan_re, "frs,fks->frk") - product(res_re, pan_im, "frs,fks->frk")
    return jnp.stack([out_re, out_im], axis=1) * scale


def make_panel(data, wavelet, live, total_shots, positions):
    rows_dev = data.shape[2]
    shots_dev = data.shape[3]
    spacing = positions // total_shots
    mask = live.astype(jnp.float32)
    observed = data * mask[None, None]
    rcv_idx = (lax.axis_index("x") * lax.axis_size("y") + lax.axis_index("y")) * lax.axis_size("zl") + lax.axis_index("zl")
    shot_idx = lax.axis_index("zh") * lax.axis_size("c") + lax.axis_index("c")
    row_ids = rcv_idx * rows_dev + lax.broadcasted_iota(jnp.int32, (rows_dev, shots_dev), 0)
    col_ids = shot_idx * shots_dev + lax.broadcasted_iota(jnp.int32, (rows_dev, shots_dev), 1)
    source = (row_ids == col_ids * spacing).astype(jnp.float32)
    panel = wavelet[:, :, None, None] * source[None, None] - observed
    return mask, observed, panel


def fine_mesh(mesh):
    n_rcv = mesh.shape["rcv"]
    n_shot = mesh.shape["shot"]
    devs = mesh.devices.reshape(2, n_shot // 2, 4, 4, n_rcv // 16)
    return Mesh(devs, ("zh", "c", "x", "y", "zl"))


def ring_gather(block, axis_name, axis, split_axis):
    n = lax.axis_size(axis_name)
    i = lax.axis_index(axis_name)
    fwd = [(s, (s + 1) % n) for s in range(n)]
    bwd = [(s, (s - 1) % n) for s in range(n)]
    left = lax.ppermute(block, axis_name, fwd)
    right = lax.ppermute(block, axis_name, bwd)
    h = block.shape[split_axis] // 2
    far_a = lax.ppermute(lax.slice_in_dim(right, 0, h, axis=split_axis), axis_name, bwd)
    far_b = lax.ppermute(lax.slice_in_dim(left, h, 2 * h, axis=split_axis), axis_name, fwd)
    shape = list(block.shape)
    shape[axis] = n
    buf = jnp.zeros(shape, block.dtype)

    def at(part, slot, offset):
        starts = [0] * len(shape)
        starts[axis] = slot
        starts[split_axis] = offset
        return lax.dynamic_update_slice(buf_ref[0], part, starts)

    buf_ref = [buf]
    for part, slot, offset in ((block, i, 0), (right, (i + 1) % n, 0), (left, (i + n - 1) % n, 0),
                               (far_a, (i + 2) % n, 0), (far_b, (i + 2) % n, h)):
        buf_ref[0] = at(part, slot, offset)
    return buf_ref[0]


def pair_gather(block, axis_name, axis):
    i = lax.axis_index(axis_name)
    other = lax.ppermute(block, axis_name, [(0, 1), (1, 0)])
    shape = list(block.shape)
    blk = shape[axis]
    shape[axis] = 2 * blk
    starts = [0] * len(shape)
    buf = jnp.zeros(shape, block.dtype)
    starts[axis] = i * blk
    buf = lax.dynamic_update_slice(buf, block, starts)
    starts[axis] = (1 - i) * blk
    return lax.dynamic_update_slice(buf, other, starts)


def local(data, impulse, wavelet, live):
    positions = impulse.shape[3]
    total_shots = data.shape[3] * lax.axis_size(SHOT)
    scale = -(total_shots ** (-0.5))
    mask, observed, panel = make_panel(data, wavelet, live, total_shots, positions)
    g = pair_gather(panel, "zl", 2)
    g_re = lax.all_gather(g[:, 0], "y", axis=1, tiled=True)
    f0, rows8, cols0 = g_re.shape
    g_re = ring_gather(g_re.reshape(f0, 1, rows8, cols0), "x", 1, 2).reshape(f0, 4 * rows8, cols0)
    f, rows2, cols = g[:, 1].shape
    gx = ring_gather(g[:, 1].reshape(f, 1, 1, rows2, cols), "x", 1, 3)
    gy = ring_gather(gx, "y", 2, 1)
    g_im = gy.reshape(f, 16 * rows2, cols)
    g = jnp.stack([g_re, g_im], axis=1)
    predicted = convolve(impulse, g)
    residual = mask[None, None] * (observed - predicted)
    lhs_re = jnp.concatenate([residual[:, 0], residual[:, 1]], axis=1) * scale
    lhs_im = jnp.concatenate([residual[:, 1], -residual[:, 0]], axis=1) * scale
    terms = product(lhs_re, g[:, 0], "frs,fks->frk") + product(lhs_im, g[:, 1], "frs,fks->frk")
    terms = terms.reshape(terms.shape[0], 2, terms.shape[1] // 2, terms.shape[2])
    gradient = lax.psum_scatter(terms, SHOT, scatter_dimension=3, tiled=True)
    return (residual, gradient)


def solution(mesh):
    m = fine_mesh(mesh)
    placed = (P(None, None, RCV, SHOT), P(None, None, RCV, None), P(), P(RCV, SHOT))
    return jax.shard_map(local, mesh=m, in_specs=placed,
                         out_specs=(P(None, None, RCV, SHOT), P(None, None, RCV, SHOT)), check_vma=False)
```

```python
import jax
import jax.numpy as jnp
from jax import lax
from jax.sharding import Mesh, PartitionSpec as P

RCV = ("x", "y", "zl")
SHOT = ("zh", "c")


def product(left, right, form):
    return jnp.einsum(form, left, right, precision=lax.Precision.HIGH, preferred_element_type=jnp.float32)


def convolve(impulse_cols, panel):
    left_re = impulse_cols[:, 0]
    left_im = impulse_cols[:, 1]
    right_re = panel[:, 0]
    right_im = panel[:, 1]
    out_re = product(left_re, right_re, "frk,fks->frs") - product(left_im, right_im, "frk,fks->frs")
    out_im = product(left_re, right_im, "frk,fks->frs") + product(left_im, right_re, "frk,fks->frs")
    return jnp.stack([out_re, out_im], axis=1)


def correlate(residual, panel, scale):
    res_re = residual[:, 0]
    res_im = residual[:, 1]
    pan_re = panel[:, 0]
    pan_im = panel[:, 1]
    out_re = product(res_re, pan_re, "frs,fks->frk") + product(res_im, pan_im, "frs,fks->frk")
    out_im = product(res_im, pan_re, "frs,fks->frk") - product(res_re, pan_im, "frs,fks->frk")
    return jnp.stack([out_re, out_im], axis=1) * scale


def make_panel(data, wavelet, live, total_shots, positions):
    rows_dev = data.shape[2]
    shots_dev = data.shape[3]
    spacing = positions // total_shots
    mask = live.astype(jnp.float32)
    observed = data * mask[None, None]
    rcv_idx = (lax.axis_index("x") * lax.axis_size("y") + lax.axis_index("y")) * lax.axis_size("zl") + lax.axis_index("zl")
    shot_idx = lax.axis_index("zh") * lax.axis_size("c") + lax.axis_index("c")
    row_ids = rcv_idx * rows_dev + lax.broadcasted_iota(jnp.int32, (rows_dev, shots_dev), 0)
    col_ids = shot_idx * shots_dev + lax.broadcasted_iota(jnp.int32, (rows_dev, shots_dev), 1)
    source = (row_ids == col_ids * spacing).astype(jnp.float32)
    panel = wavelet[:, :, None, None] * source[None, None] - observed
    return mask, observed, panel


def fine_mesh(mesh):
    n_rcv = mesh.shape["rcv"]
    n_shot = mesh.shape["shot"]
    devs = mesh.devices.reshape(2, n_shot // 2, 4, 4, n_rcv // 16)
    return Mesh(devs, ("zh", "c", "x", "y", "zl"))


def ring_near(block, axis_name):
    n = lax.axis_size(axis_name)
    fwd = [(s, (s + 1) % n) for s in range(n)]
    bwd = [(s, (s - 1) % n) for s in range(n)]
    return lax.ppermute(block, axis_name, fwd), lax.ppermute(block, axis_name, bwd)


def ring_far(block, left, right, axis_name, axis, split_axis):
    n = lax.axis_size(axis_name)
    i = lax.axis_index(axis_name)
    fwd = [(s, (s + 1) % n) for s in range(n)]
    bwd = [(s, (s - 1) % n) for s in range(n)]
    h = block.shape[split_axis] // 2
    far_a = lax.ppermute(lax.slice_in_dim(right, 0, h, axis=split_axis), axis_name, bwd)
    far_b = lax.ppermute(lax.slice_in_dim(left, h, 2 * h, axis=split_axis), axis_name, fwd)
    shape = list(block.shape)
    shape[axis] = n
    buf = jnp.zeros(shape, block.dtype)
    for part, slot, offset in ((block, i, 0), (right, (i + 1) % n, 0), (left, (i + n - 1) % n, 0),
                               (far_a, (i + 2) % n, 0), (far_b, (i + 2) % n, h)):
        starts = [0] * len(shape)
        starts[axis] = slot
        starts[split_axis] = offset
        buf = lax.dynamic_update_slice(buf, part, starts)
    return buf


def ring_gather(block, axis_name, axis, split_axis):
    left, right = ring_near(block, axis_name)
    return ring_far(block, left, right, axis_name, axis, split_axis)


def pair_gather(block, axis_name, axis):
    i = lax.axis_index(axis_name)
    other = lax.ppermute(block, axis_name, [(0, 1), (1, 0)])
    shape = list(block.shape)
    blk = shape[axis]
    shape[axis] = 2 * blk
    starts = [0] * len(shape)
    buf = jnp.zeros(shape, block.dtype)
    starts[axis] = i * blk
    buf = lax.dynamic_update_slice(buf, block, starts)
    starts[axis] = (1 - i) * blk
    return lax.dynamic_update_slice(buf, other, starts)


def local(data, impulse, wavelet, live):
    positions = impulse.shape[3]
    total_shots = data.shape[3] * lax.axis_size(SHOT)
    scale = -(total_shots ** (-0.5))
    mask, observed, panel = make_panel(data, wavelet, live, total_shots, positions)
    g = pair_gather(panel, "zl", 2)
    g_re = lax.all_gather(g[:, 0], "y", axis=1, tiled=True)
    f0, rows8, cols0 = g_re.shape
    f, rows2, cols = g[:, 1].shape
    gx = ring_gather(g[:, 1].reshape(f, 1, 1, rows2, cols), "x", 1, 3)
    b_re = g_re.reshape(f0, 1, rows8, cols0)
    l_re, r_re = ring_near(b_re, "x")
    l_im, r_im = ring_near(gx, "y")
    l_re, r_re, l_im, r_im = lax.optimization_barrier((l_re, r_re, l_im, r_im))
    g_re = ring_far(b_re, l_re, r_re, "x", 1, 2).reshape(f0, 4 * rows8, cols0)
    g_im = ring_far(gx, l_im, r_im, "y", 2, 1).reshape(f, 16 * rows2, cols)
    g = jnp.stack([g_re, g_im], axis=1)
    predicted = convolve(impulse, g)
    residual = mask[None, None] * (observed - predicted)
    lhs_re = jnp.concatenate([residual[:, 0], residual[:, 1]], axis=1) * scale
    lhs_im = jnp.concatenate([residual[:, 1], -residual[:, 0]], axis=1) * scale
    terms = product(lhs_re, g[:, 0], "frs,fks->frk") + product(lhs_im, g[:, 1], "frs,fks->frk")
    terms = terms.reshape(terms.shape[0], 2, terms.shape[1] // 2, terms.shape[2])
    gradient = lax.psum_scatter(terms, SHOT, scatter_dimension=3, tiled=True)
    return (residual, gradient)


def solution(mesh):
    m = fine_mesh(mesh)
    placed = (P(None, None, RCV, SHOT), P(None, None, RCV, None), P(), P(RCV, SHOT))
    return jax.shard_map(local, mesh=m, in_specs=placed,
                         out_specs=(P(None, None, RCV, SHOT), P(None, None, RCV, SHOT)), check_vma=False)
```

```python
import jax
import jax.numpy as jnp
from jax import lax
from jax.sharding import Mesh, PartitionSpec as P

RCV = ("x", "y", "zl")
SHOT = ("zh", "c")


def product(left, right, form):
    return jnp.einsum(form, left, right, precision=lax.Precision.HIGH, preferred_element_type=jnp.float32)


def convolve(impulse_cols, panel):
    left_re = impulse_cols[:, 0]
    left_im = impulse_cols[:, 1]
    right_re = panel[:, 0]
    right_im = panel[:, 1]
    out_re = product(left_re, right_re, "frk,fks->frs") - product(left_im, right_im, "frk,fks->frs")
    out_im = product(left_re, right_im, "frk,fks->frs") + product(left_im, right_re, "frk,fks->frs")
    return jnp.stack([out_re, out_im], axis=1)


def correlate(residual, panel, scale):
    res_re = residual[:, 0]
    res_im = residual[:, 1]
    pan_re = panel[:, 0]
    pan_im = panel[:, 1]
    out_re = product(res_re, pan_re, "frs,fks->frk") + product(res_im, pan_im, "frs,fks->frk")
    out_im = product(res_im, pan_re, "frs,fks->frk") - product(res_re, pan_im, "frs,fks->frk")
    return jnp.stack([out_re, out_im], axis=1) * scale


def make_panel(data, wavelet, live, total_shots, positions):
    rows_dev = data.shape[2]
    shots_dev = data.shape[3]
    spacing = positions // total_shots
    mask = live.astype(jnp.float32)
    observed = data * mask[None, None]
    rcv_idx = (lax.axis_index("x") * lax.axis_size("y") + lax.axis_index("y")) * lax.axis_size("zl") + lax.axis_index("zl")
    shot_idx = lax.axis_index("zh") * lax.axis_size("c") + lax.axis_index("c")
    row_ids = rcv_idx * rows_dev + lax.broadcasted_iota(jnp.int32, (rows_dev, shots_dev), 0)
    col_ids = shot_idx * shots_dev + lax.broadcasted_iota(jnp.int32, (rows_dev, shots_dev), 1)
    source = (row_ids == col_ids * spacing).astype(jnp.float32)
    panel = wavelet[:, :, None, None] * source[None, None] - observed
    return mask, observed, panel


def fine_mesh(mesh):
    n_rcv = mesh.shape["rcv"]
    n_shot = mesh.shape["shot"]
    devs = mesh.devices.reshape(2, n_shot // 2, 4, 4, n_rcv // 16)
    return Mesh(devs, ("zh", "c", "x", "y", "zl"))


def ring_near(block, axis_name):
    n = lax.axis_size(axis_name)
    fwd = [(s, (s + 1) % n) for s in range(n)]
    bwd = [(s, (s - 1) % n) for s in range(n)]
    return lax.ppermute(block, axis_name, fwd), lax.ppermute(block, axis_name, bwd)


def ring_far(block, left, right, axis_name, axis, split_axis):
    n = lax.axis_size(axis_name)
    i = lax.axis_index(axis_name)
    fwd = [(s, (s + 1) % n) for s in range(n)]
    bwd = [(s, (s - 1) % n) for s in range(n)]
    h = block.shape[split_axis] // 2
    far_a = lax.ppermute(lax.slice_in_dim(right, 0, h, axis=split_axis), axis_name, bwd)
    far_b = lax.ppermute(lax.slice_in_dim(left, h, 2 * h, axis=split_axis), axis_name, fwd)
    shape = list(block.shape)
    shape[axis] = n
    buf = jnp.zeros(shape, block.dtype)
    for part, slot, offset in ((block, i, 0), (right, (i + 1) % n, 0), (left, (i + n - 1) % n, 0),
                               (far_a, (i + 2) % n, 0), (far_b, (i + 2) % n, h)):
        starts = [0] * len(shape)
        starts[axis] = slot
        starts[split_axis] = offset
        buf = lax.dynamic_update_slice(buf, part, starts)
    return buf


def ring_gather(block, axis_name, axis, split_axis):
    left, right = ring_near(block, axis_name)
    return ring_far(block, left, right, axis_name, axis, split_axis)


def pair_gather(block, axis_name, axis):
    i = lax.axis_index(axis_name)
    other = lax.ppermute(block, axis_name, [(0, 1), (1, 0)])
    shape = list(block.shape)
    blk = shape[axis]
    shape[axis] = 2 * blk
    starts = [0] * len(shape)
    buf = jnp.zeros(shape, block.dtype)
    starts[axis] = i * blk
    buf = lax.dynamic_update_slice(buf, block, starts)
    starts[axis] = (1 - i) * blk
    return lax.dynamic_update_slice(buf, other, starts)


def local(data, impulse, wavelet, live):
    positions = impulse.shape[3]
    total_shots = data.shape[3] * lax.axis_size(SHOT)
    scale = -(total_shots ** (-0.5))
    mask, observed, panel = make_panel(data, wavelet, live, total_shots, positions)
    g_re = pair_gather(panel[:, 0], "zl", 1)
    g_re = lax.all_gather(g_re, "y", axis=1, tiled=True)
    f0, rows8, cols0 = g_re.shape
    f, rows1, cols = panel[:, 1].shape
    gx = ring_gather(panel[:, 1].reshape(f, 1, 1, 1, rows1, cols), "x", 1, 4)
    gx = pair_gather(gx, "zl", 3)
    b_re = g_re.reshape(f0, 1, rows8, cols0)
    l_re, r_re = ring_near(b_re, "x")
    l_im, r_im = ring_near(gx, "y")
    l_re, r_re, l_im, r_im = lax.optimization_barrier((l_re, r_re, l_im, r_im))
    g_re = ring_far(b_re, l_re, r_re, "x", 1, 2).reshape(f0, 4 * rows8, cols0)
    g_im = ring_far(gx, l_im, r_im, "y", 2, 1).reshape(f, 32 * rows1, cols)
    g = jnp.stack([g_re, g_im], axis=1)
    predicted = convolve(impulse, g)
    residual = mask[None, None] * (observed - predicted)
    lhs_re = jnp.concatenate([residual[:, 0], residual[:, 1]], axis=1) * scale
    lhs_im = jnp.concatenate([residual[:, 1], -residual[:, 0]], axis=1) * scale
    terms = product(lhs_re, g[:, 0], "frs,fks->frk") + product(lhs_im, g[:, 1], "frs,fks->frk")
    terms = terms.reshape(terms.shape[0], 2, terms.shape[1] // 2, terms.shape[2])
    gradient = lax.psum_scatter(terms, SHOT, scatter_dimension=3, tiled=True)
    return (residual, gradient)


def solution(mesh):
    m = fine_mesh(mesh)
    placed = (P(None, None, RCV, SHOT), P(None, None, RCV, None), P(), P(RCV, SHOT))
    return jax.shard_map(local, mesh=m, in_specs=placed,
                         out_specs=(P(None, None, RCV, SHOT), P(None, None, RCV, SHOT)), check_vma=False)
```
